512 devices in a mesh: tm: 16 (over y, core), pre: 32 (over z, x).
Axes of the slice: x: 4, y: 8, z: 8, core: 2. Of those that a mesh axis runs over, the one named last changes fastest.
Arguments:
- spikes: int32 [3072, 16384], P('tm', 'pre'), may hold values from 0 to 1
- trace_decay: float32 [16384], P('pre'), may hold values from 0.96 to 1
- pseudo_deriv: bfloat16 [3072, 16384], P('pre', 'tm'), may hold values from 0 to 0.29882812
- readout_weight: bfloat16 [16384, 512], P('pre'), may hold values from -2 to 2
- feedback_weight: bfloat16 [16384, 512], P('tm'), may hold values from -6 to 6
- targets: int32 [3072], P('tm'), may hold values from 0 to 511
Outputs:
- gradient: float32 [16384, 16384], P('pre', 'tm')
The draws below stay inside these ranges and needn't reach their ends.
All inputs are finite; a program needn't handle non-finite values.
Results may differ from the reference program's by a relative error of at most 0.0022.
Values may be sent and summed in bfloat16 or wider, within the bound.
No kernel may reach another device: no remote copies, remote signals or barrier semaphores. Data moves between devices by JAX's collectives and lax.ppermute only.
A program may use at most 64 MiB of HBM per device.

```python
import math
import jax
import jax.numpy as jnp
from jax import lax

N = 16384
C = 512
STEPS = 3072


def draw_spikes(key, part):
    level_key = jax.random.fold_in(key, 11)
    spike_key = jax.random.fold_in(key, 12)
    levels = jax.random.randint(level_key, (STEPS, 1), 1, 9)
    dice_rolls = jax.random.randint(spike_key, (STEPS, N), 0, 32)
    return (dice_rolls < levels).astype(jnp.int32)


def draw_trace_decay(key, part):
    pick_key = jax.random.fold_in(key, 21)
    rate_key = jax.random.fold_in(key, 22)
    share = 0.5
    low_slow = math.log(1.0 / (8.0 * STEPS))
    high_slow = math.log(1.0 / (2.0 * STEPS))
    high_fast = math.log(1.0 / 30.0)
    chooser = jax.random.uniform(pick_key, (N,), jnp.float32)
    unit_draw = jax.random.uniform(rate_key, (N,), jnp.float32)
    slow_rate = jnp.exp(low_slow + (high_slow - low_slow) * unit_draw)
    fast_rate = jnp.exp(high_slow + (high_fast - high_slow) * unit_draw)
    leak_rate = jnp.where(chooser < share, slow_rate, fast_rate)
    return (1.0 - leak_rate).astype(jnp.float32)


def draw_readout_weight(key, part):
    spread = 3.0 / math.sqrt(N * 9 // 64)
    base_draw = jnp.clip(jax.random.normal(key, (N, C), jnp.float32), -4.0, 4.0) * spread
    return jnp.clip(base_draw, -2.0, 2.0).astype(jnp.bfloat16)


def plant(entries, stream_key, low, high):
    longest = entries.shape.index(max(entries.shape))
    spots = []
    for shift in (0, 1):
        where = [jax.random.randint(jax.random.fold_in(stream_key, axis), (), 0, length) for axis, length in enumerate(entries.shape)]
        where[longest] = (where[longest] + shift) % entries.shape[longest]
        spots.append(tuple(where))
    return entries.at[spots[0]].set(low).at[spots[1]].set(high)


def shard_levels(key, extent, shards, least, top_value):
    level, own = 1.0, jax.random.fold_in(key, 6)
    for dim, shards_of in shards:
        steps = jnp.exp(jax.random.uniform(jax.random.fold_in(own, dim), (shards_of,), jnp.float32, least / len(shards), top_value / len(shards)))
        level = level * jnp.repeat(steps, extent[dim] // shards_of).reshape([-1 if axis == dim else 1 for axis in range(len(extent))])
    return level


def noise(stream_key, shape, width, limit, cuts=(), kind=jnp.bfloat16):
    result = jax.random.normal(stream_key, shape, jnp.float32) * width
    if len(cuts) > 0:
        result = shard_levels(stream_key, shape, cuts, -0.22, 0.18) * result
    return jnp.clip(result, min=-limit, max=limit).astype(kind)


def setup_inputs(seed: int = 0) -> dict:
    keys = jax.random.split(jax.random.key(seed), 7)
    return {
        "spikes": draw_spikes(jax.random.fold_in(keys[6], 71), 0),
        "trace_decay": draw_trace_decay(jax.random.fold_in(keys[6], 71), 0),
        "pseudo_deriv": jnp.clip(0.29882812 * jax.random.uniform(keys[2], (STEPS, N), jnp.float32) ** shard_levels(keys[2], (STEPS, N), ((0, 32), (1, 16)), -0.2, 0.2), 0.0, 0.29882812).astype(jnp.bfloat16),
        "readout_weight": draw_readout_weight(jax.random.fold_in(keys[6], 71), 0),
        "feedback_weight": noise(keys[4], (N, C), 1.0, 6.0, ((0, 16),)),
        "targets": plant(jax.random.randint(keys[5], (STEPS,), 0, C), jax.random.fold_in(keys[5], 1), 0, C - 1).astype(jnp.int32),
    }


def reference(spikes, trace_decay, pseudo_deriv, readout_weight, feedback_weight, targets):
    spike_float = spikes.astype(jnp.bfloat16).astype(jnp.float32)
    logits = jnp.dot(spike_float, readout_weight.astype(jnp.float32), precision=lax.Precision.HIGHEST, preferred_element_type=jnp.float32)
    class_prob = jax.nn.softmax(logits, axis=-1)
    classes = jnp.arange(logits.shape[1], dtype=jnp.int32)
    onehot = (targets[:, None] == classes[None, :]).astype(jnp.float32)
    errors = (class_prob - onehot).astype(jnp.bfloat16)
    signal = lax.dot_general(errors.astype(jnp.float32), feedback_weight.astype(jnp.float32), (((1,), (1,)), ((), ())), precision=lax.Precision.HIGHEST, preferred_element_type=jnp.float32)
    weighted = (signal * pseudo_deriv.astype(jnp.float32)).astype(jnp.bfloat16)

    def advance(state, column):
        fresh = trace_decay * state + (1.0 - trace_decay) * column
        return fresh, fresh.astype(jnp.bfloat16)

    final_state, trace_bf = lax.scan(advance, jnp.zeros(trace_decay.shape, jnp.float32), spike_float)
    gradient = lax.dot_general(trace_bf.astype(jnp.float32), weighted.astype(jnp.float32), (((0,), (0,)), ((), ())), precision=lax.Precision.HIGHEST, preferred_element_type=jnp.float32)
    return gradient
```

```python
import jax
import jax.numpy as jnp
from jax import lax
from jax.sharding import PartitionSpec as P


def combine_pairs(earlier, later):
    return (earlier[0] * later[0], later[1] + later[0] * earlier[1])


def local_traces(spikes, decays):
    factor = jnp.broadcast_to(decays[None, :], spikes.shape)
    source = (1.0 - decays)[None, :] * spikes.astype(jnp.float32)
    return lax.associative_scan(combine_pairs, (factor, source), axis=0)


def owned_errors(spikes, readout_weight, targets):
    npre = lax.axis_size("pre")
    b = lax.axis_index("pre")
    partial_logits = jnp.dot(
        spikes.astype(jnp.bfloat16), readout_weight, preferred_element_type=jnp.float32
    )
    rows = partial_logits.shape[0] // npre
    pieces = lax.all_to_all(partial_logits, "pre", 0, 0, tiled=True)
    logits = pieces.reshape(npre, rows, -1).sum(0)
    class_prob = jax.nn.softmax(logits, axis=-1)
    classes = lax.broadcasted_iota(jnp.int32, logits.shape, 1)
    mine = lax.dynamic_slice_in_dim(targets, b * rows, rows, 0)
    onehot = (mine[:, None] == classes).astype(jnp.float32)
    return (class_prob - onehot).astype(jnp.bfloat16)


def route_errors(errors, ntm, npre, deriv_rows):
    rows = errors.shape[0]
    tstep = rows * npre
    per = deriv_rows // rows
    perm = []
    for a in range(ntm):
        for b in range(npre):
            start = tstep * a + rows * b
            dst_b = start // deriv_rows
            dst_a = (start % deriv_rows) // rows
            perm.append((a * npre + b, dst_a * npre + dst_b))
    moved = lax.ppermute(errors, ("tm", "pre"), perm)
    assert per == ntm
    return lax.all_gather(moved, "tm", axis=0, tiled=True)


def ring_gather(block, axis, count):
    index = lax.axis_index(axis)
    fwd = [(i, (i + 1) % count) for i in range(count)]
    bwd = [(i, (i - 1) % count) for i in range(count)]
    out = jnp.zeros((count,) + block.shape, block.dtype)
    out = lax.dynamic_update_slice_in_dim(out, block[None], index, 0)
    f = block
    b = block
    for s in range(1, count // 2 + 1):
        f = lax.ppermute(f, axis, fwd)
        out = lax.dynamic_update_slice_in_dim(out, f[None], (index - s) % count, 0)
        if s < count - count // 2:
            b = lax.ppermute(b, axis, bwd)
            out = lax.dynamic_update_slice_in_dim(out, b[None], (index + s) % count, 0)
    return out.reshape((count * block.shape[0],) + block.shape[1:])


def shards(spikes, trace_decay, pseudo_deriv, readout_weight, feedback_weight, targets):
    ntm = lax.axis_size("tm")
    npre = lax.axis_size("pre")
    a = lax.axis_index("tm")

    errors = owned_errors(spikes, readout_weight, targets)
    err_rows = route_errors(errors, ntm, npre, pseudo_deriv.shape[0])
    signal = lax.dot_general(
        err_rows, feedback_weight, (((1,), (1,)), ((), ())), preferred_element_type=jnp.float32
    )
    weighted = (signal * pseudo_deriv.astype(jnp.float32)).astype(jnp.bfloat16)
    weighted_all = lax.all_gather(weighted, "pre", axis=0, tiled=True)

    powers, states = local_traces(spikes, trace_decay)
    ends = lax.all_gather(states[-1], "tm", axis=0)
    span = powers[-1]

    def step(k, carry):
        return jnp.where(k < a, span * carry + ends[k], carry)

    incoming = lax.fori_loop(0, ntm, step, jnp.zeros_like(trace_decay))
    traces = (states + powers * incoming[None, :]).astype(jnp.bfloat16)
    traces_all = ring_gather(traces, "tm", ntm)

    return lax.dot_general(
        traces_all, weighted_all, (((0,), (0,)), ((), ())), preferred_element_type=jnp.float32
    )


def solution(mesh):
    placed = (P("tm", "pre"), P("pre"), P("pre", "tm"), P("pre", None), P("tm", None), P("tm"))
    return jax.shard_map(
        shards, mesh=mesh, in_specs=placed, out_specs=P("pre", "tm"), check_vma=False
    )
```

```python
import jax
import jax.numpy as jnp
from jax import lax
from jax.sharding import PartitionSpec as P


def combine_pairs(earlier, later):
    return (earlier[0] * later[0], later[1] + later[0] * earlier[1])


def local_traces(spikes, decays):
    factor = jnp.broadcast_to(decays[None, :], spikes.shape)
    source = (1.0 - decays)[None, :] * spikes.astype(jnp.float32)
    return lax.associative_scan(combine_pairs, (factor, source), axis=0)


def owned_errors(spikes, readout_weight, targets):
    npre = lax.axis_size("pre")
    b = lax.axis_index("pre")
    partial_logits = jnp.dot(
        spikes.astype(jnp.bfloat16), readout_weight, preferred_element_type=jnp.float32
    )
    rows = partial_logits.shape[0] // npre
    pieces = lax.all_to_all(partial_logits, "pre", 0, 0, tiled=True)
    logits = pieces.reshape(npre, rows, -1).sum(0)
    class_prob = jax.nn.softmax(logits, axis=-1)
    classes = lax.broadcasted_iota(jnp.int32, logits.shape, 1)
    mine = lax.dynamic_slice_in_dim(targets, b * rows, rows, 0)
    onehot = (mine[:, None] == classes).astype(jnp.float32)
    return (class_prob - onehot).astype(jnp.bfloat16)


def route_errors(errors, ntm, npre, deriv_rows):
    rows = errors.shape[0]
    tstep = rows * npre
    perm = []
    for a in range(ntm):
        for b in range(npre):
            start = tstep * a + rows * b
            dst_b = start // deriv_rows
            dst_a = (start % deriv_rows) // rows
            perm.append((a * npre + b, dst_a * npre + dst_b))
    moved = lax.ppermute(errors, ("tm", "pre"), perm)
    return doubling_gather(moved, "tm", ntm)


def doubling_gather(block, axis, count):
    index = lax.axis_index(axis)
    have = block
    span = 1
    while span < count:
        pairs = [(i, i ^ span) for i in range(count)]
        got = lax.ppermute(have, axis, pairs)
        upper = (index & span) != 0
        have = jnp.where(upper, jnp.concatenate([got, have], 0), jnp.concatenate([have, got], 0))
        span *= 2
    return have


def exclusive_carry(end_state, span_power, axis, count):
    x = lax.ppermute(end_state, axis, [(i, i + 1) for i in range(count - 1)])
    power = span_power
    shift = 1
    while shift < count:
        got = lax.ppermute(x, axis, [(i, i + shift) for i in range(count - shift)])
        x = x + power * got
        power = power * power
        shift *= 2
    return x


def ring_gather(block, axis, count):
    index = lax.axis_index(axis)
    fwd = [(i, (i + 1) % count) for i in range(count)]
    bwd = [(i, (i - 1) % count) for i in range(count)]
    out = jnp.zeros((count,) + block.shape, block.dtype)
    out = lax.dynamic_update_slice_in_dim(out, block[None], index, 0)
    f = block
    b = block
    for s in range(1, count // 2 + 1):
        f = lax.ppermute(f, axis, fwd)
        out = lax.dynamic_update_slice_in_dim(out, f[None], (index - s) % count, 0)
        if s < count - count // 2:
            b = lax.ppermute(b, axis, bwd)
            out = lax.dynamic_update_slice_in_dim(out, b[None], (index + s) % count, 0)
    return out.reshape((count * block.shape[0],) + block.shape[1:])


def shards(spikes, trace_decay, pseudo_deriv, readout_weight, feedback_weight, targets):
    ntm = lax.axis_size("tm")
    npre = lax.axis_size("pre")

    errors = owned_errors(spikes, readout_weight, targets)
    err_rows = route_errors(errors, ntm, npre, pseudo_deriv.shape[0])
    signal = lax.dot_general(
        err_rows, feedback_weight, (((1,), (1,)), ((), ())), preferred_element_type=jnp.float32
    )
    weighted = (signal * pseudo_deriv.astype(jnp.float32)).astype(jnp.bfloat16)
    weighted_all = lax.all_gather(weighted, "pre", axis=0, tiled=True)

    powers, states = local_traces(spikes, trace_decay)
    incoming = exclusive_carry(states[-1], powers[-1], "tm", ntm)
    traces = (states + powers * incoming[None, :]).astype(jnp.bfloat16)
    traces_all = ring_gather(traces, "tm", ntm)

    return lax.dot_general(
        traces_all, weighted_all, (((0,), (0,)), ((), ())), preferred_element_type=jnp.float32
    )


def solution(mesh):
    placed = (P("tm", "pre"), P("pre"), P("pre", "tm"), P("pre", None), P("tm", None), P("tm"))
    return jax.shard_map(
        shards, mesh=mesh, in_specs=placed, out_specs=P("pre", "tm"), check_vma=False
    )
```

```python
import jax
import jax.numpy as jnp
from jax import lax
from jax.sharding import PartitionSpec as P

NZ = 8


def combine_pairs(earlier, later):
    return (earlier[0] * later[0], later[1] + later[0] * earlier[1])


def local_traces(spikes, decays):
    factor = jnp.broadcast_to(decays[None, :], spikes.shape)
    source = (1.0 - decays)[None, :] * spikes.astype(jnp.float32)
    return lax.associative_scan(combine_pairs, (factor, source), axis=0)


def owned_errors(spikes, readout_weight, targets):
    npre = lax.axis_size("pre")
    b = lax.axis_index("pre")
    partial_logits = jnp.dot(
        spikes.astype(jnp.bfloat16), readout_weight, preferred_element_type=jnp.float32
    )
    rows = partial_logits.shape[0] // npre
    pieces = lax.all_to_all(partial_logits, "pre", 0, 0, tiled=True)
    logits = pieces.reshape(npre, rows, -1).sum(0)
    class_prob = jax.nn.softmax(logits, axis=-1)
    classes = lax.broadcasted_iota(jnp.int32, logits.shape, 1)
    mine = lax.dynamic_slice_in_dim(targets, b * rows, rows, 0)
    onehot = (mine[:, None] == classes).astype(jnp.float32)
    return (class_prob - onehot).astype(jnp.bfloat16)


def route_errors(errors, ntm, npre, deriv_rows):
    rows = errors.shape[0]
    tstep = rows * npre
    per = deriv_rows // rows
    perm = []
    for a in range(ntm):
        for b in range(npre):
            start = tstep * a + rows * b
            dst_b = start // deriv_rows
            dst_a = (start % deriv_rows) // rows
            perm.append((a * npre + b, dst_a * npre + dst_b))
    moved = lax.ppermute(errors, ("tm", "pre"), perm)
    assert per == ntm
    return lax.all_gather(moved, "tm", axis=0, tiled=True)


def ring_gather(block, axis, count):
    index = lax.axis_index(axis)
    fwd = [(i, (i + 1) % count) for i in range(count)]
    bwd = [(i, (i - 1) % count) for i in range(count)]
    out = jnp.zeros((count,) + block.shape, block.dtype)
    out = lax.dynamic_update_slice_in_dim(out, block[None], index, 0)
    f = block
    b = block
    for s in range(1, count // 2 + 1):
        f = lax.ppermute(f, axis, fwd)
        out = lax.dynamic_update_slice_in_dim(out, f[None], (index - s) % count, 0)
        if s < count - count // 2:
            b = lax.ppermute(b, axis, bwd)
            out = lax.dynamic_update_slice_in_dim(out, b[None], (index + s) % count, 0)
    return out.reshape((count * block.shape[0],) + block.shape[1:])


def plane_gather(block, nz, nx):
    b = lax.axis_index("pre")
    z = b // nx
    x = b % nx
    xf = [(zz * nx + xx, zz * nx + (xx + 1) % nx) for zz in range(nz) for xx in range(nx)]
    xb = [(zz * nx + xx, zz * nx + (xx - 1) % nx) for zz in range(nz) for xx in range(nx)]
    zf = [(zz * nx + xx, ((zz + 1) % nz) * nx + xx) for zz in range(nz) for xx in range(nx)]
    zb = [(zz * nx + xx, ((zz - 1) % nz) * nx + xx) for zz in range(nz) for xx in range(nx)]
    group = jnp.zeros((nx,) + block.shape, block.dtype)
    group = lax.dynamic_update_slice_in_dim(group, block[None], x, 0)
    f = block
    r = block
    for s in range(1, nx // 2 + 1):
        f = lax.ppermute(f, "pre", xf)
        group = lax.dynamic_update_slice_in_dim(group, f[None], (x - s) % nx, 0)
        if s < nx - nx // 2:
            r = lax.ppermute(r, "pre", xb)
            group = lax.dynamic_update_slice_in_dim(group, r[None], (x + s) % nx, 0)
    out = jnp.zeros((nz,) + group.shape, block.dtype)
    out = lax.dynamic_update_slice_in_dim(out, group[None], z, 0)
    f = group
    r = group
    for s in range(1, nz // 2 + 1):
        f = lax.ppermute(f, "pre", zf)
        out = lax.dynamic_update_slice_in_dim(out, f[None], (z - s) % nz, 0)
        if s < nz - nz // 2:
            r = lax.ppermute(r, "pre", zb)
            out = lax.dynamic_update_slice_in_dim(out, r[None], (z + s) % nz, 0)
    return out.reshape((nz * nx * block.shape[0],) + block.shape[1:])


def shards(spikes, trace_decay, pseudo_deriv, readout_weight, feedback_weight, targets):
    ntm = lax.axis_size("tm")
    npre = lax.axis_size("pre")
    a = lax.axis_index("tm")

    errors = owned_errors(spikes, readout_weight, targets)
    err_rows = route_errors(errors, ntm, npre, pseudo_deriv.shape[0])
    signal = lax.dot_general(
        err_rows, feedback_weight, (((1,), (1,)), ((), ())), preferred_element_type=jnp.float32
    )
    weighted = (signal * pseudo_deriv.astype(jnp.float32)).astype(jnp.bfloat16)
    half = weighted.shape[1] // 2
    left_all = lax.all_gather(weighted[:, :half], "pre", axis=0, tiled=True)
    right_all = plane_gather(weighted[:, half:], NZ, npre // NZ)

    powers, states = local_traces(spikes, trace_decay)
    ends = lax.all_gather(states[-1], "tm", axis=0)
    span = powers[-1]

    def step(k, carry):
        return jnp.where(k < a, span * carry + ends[k], carry)

    incoming = lax.fori_loop(0, ntm, step, jnp.zeros_like(trace_decay))
    traces = (states + powers * incoming[None, :]).astype(jnp.bfloat16)
    traces_all = ring_gather(traces, "tm", ntm)

    left = outer_sum(traces_all, left_all)
    right = outer_sum(traces_all, right_all)
    return jnp.concatenate([left, right], 1)


def outer_sum(left_rows, right_rows):
    return lax.dot_general(
        left_rows, right_rows, (((0,), (0,)), ((), ())), preferred_element_type=jnp.float32
    )


def solution(mesh):
    placed = (P("tm", "pre"), P("pre"), P("pre", "tm"), P("pre", None), P("tm", None), P("tm"))
    return jax.shard_map(
        shards, mesh=mesh, in_specs=placed, out_specs=P("pre", "tm"), check_vma=False
    )
```

```python
import jax
import jax.numpy as jnp
from jax import lax
from jax.sharding import PartitionSpec as P

NZ = 8


def combine_pairs(earlier, later):
    return (earlier[0] * later[0], later[1] + later[0] * earlier[1])


def local_traces(spikes, decays):
    factor = jnp.broadcast_to(decays[None, :], spikes.shape)
    source = (1.0 - decays)[None, :] * spikes.astype(jnp.float32)
    return lax.associative_scan(combine_pairs, (factor, source), axis=0)


def owned_errors(spikes, readout_weight, targets):
    npre = lax.axis_size("pre")
    b = lax.axis_index("pre")
    partial_logits = jnp.dot(
        spikes.astype(jnp.bfloat16), readout_weight, preferred_element_type=jnp.float32
    )
    rows = partial_logits.shape[0] // npre
    pieces = lax.all_to_all(partial_logits, "pre", 0, 0, tiled=True)
    logits = pieces.reshape(npre, rows, -1).sum(0)
    class_prob = jax.nn.softmax(logits, axis=-1)
    classes = lax.broadcasted_iota(jnp.int32, logits.shape, 1)
    mine = lax.dynamic_slice_in_dim(targets, b * rows, rows, 0)
    onehot = (mine[:, None] == classes).astype(jnp.float32)
    return (class_prob - onehot).astype(jnp.bfloat16)


def route_errors(errors, ntm, npre, deriv_rows):
    rows = errors.shape[0]
    tstep = rows * npre
    per = deriv_rows // rows
    perm = []
    for a in range(ntm):
        for b in range(npre):
            start = tstep * a + rows * b
            dst_b = start // deriv_rows
            dst_a = (start % deriv_rows) // rows
            perm.append((a * npre + b, dst_a * npre + dst_b))
    moved = lax.ppermute(errors, ("tm", "pre"), perm)
    assert per == ntm
    return lax.all_gather(moved, "tm", axis=0, tiled=True)


def ring_stage(block, coord, count, fwd, bwd):
    out = jnp.zeros((count,) + block.shape, block.dtype)
    out = lax.dynamic_update_slice_in_dim(out, block[None], coord, 0)
    f = block
    r = block
    for s in range(1, count // 2 + 1):
        f = lax.ppermute(f, "pre", fwd)
        out = lax.dynamic_update_slice_in_dim(out, f[None], (coord - s) % count, 0)
        if s < count - count // 2:
            r = lax.ppermute(r, "pre", bwd)
            out = lax.dynamic_update_slice_in_dim(out, r[None], (coord + s) % count, 0)
    return out


def plane_gather(block, nz, nx):
    b = lax.axis_index("pre")
    z = b // nx
    x = b % nx
    xf = [(zz * nx + xx, zz * nx + (xx + 1) % nx) for zz in range(nz) for xx in range(nx)]
    xb = [(zz * nx + xx, zz * nx + (xx - 1) % nx) for zz in range(nz) for xx in range(nx)]
    zf = [(zz * nx + xx, ((zz + 1) % nz) * nx + xx) for zz in range(nz) for xx in range(nx)]
    zb = [(zz * nx + xx, ((zz - 1) % nz) * nx + xx) for zz in range(nz) for xx in range(nx)]
    half = block.shape[1] // 2
    rows = nz * nx * block.shape[0]
    first = ring_stage(ring_stage(block[:, :half], x, nx, xf, xb), z, nz, zf, zb)
    second = ring_stage(ring_stage(block[:, half:], z, nz, zf, zb), x, nx, xf, xb)
    second = jnp.swapaxes(second, 0, 1)
    return first.reshape(rows, half), second.reshape(rows, -1)


def shards(spikes, trace_decay, pseudo_deriv, readout_weight, feedback_weight, targets):
    ntm = lax.axis_size("tm")
    npre = lax.axis_size("pre")
    a = lax.axis_index("tm")

    errors = owned_errors(spikes, readout_weight, targets)
    err_rows = route_errors(errors, ntm, npre, pseudo_deriv.shape[0])
    signal = lax.dot_general(
        err_rows, feedback_weight, (((1,), (1,)), ((), ())), preferred_element_type=jnp.float32
    )
    weighted = (signal * pseudo_deriv.astype(jnp.float32)).astype(jnp.bfloat16)
    assert npre % NZ == 0
    left_all, right_all = plane_gather(weighted, NZ, npre // NZ)

    powers, states = local_traces(spikes, trace_decay)
    ends = lax.all_gather(states[-1], "tm", axis=0)
    span = powers[-1]

    def step(k, carry):
        return jnp.where(k < a, span * carry + ends[k], carry)

    incoming = lax.fori_loop(0, ntm, step, jnp.zeros_like(trace_decay))
    traces = (states + powers * incoming[None, :]).astype(jnp.bfloat16)
    traces_all = lax.all_gather(traces, "tm", axis=0, tiled=True)
    left = outer_sum(traces_all, left_all)
    right = outer_sum(traces_all, right_all)
    return jnp.concatenate([left, right], 1)


def outer_sum(left_rows, right_rows):
    return lax.dot_general(
        left_rows, right_rows, (((0,), (0,)), ((), ())), preferred_element_type=jnp.float32
    )


def solution(mesh):
    placed = (P("tm", "pre"), P("pre"), P("pre", "tm"), P("pre", None), P("tm", None), P("tm"))
    return jax.shard_map(
        shards, mesh=mesh, in_specs=placed, out_specs=P("pre", "tm"), check_vma=False
    )
```

```python
import jax
import jax.numpy as jnp
from jax import lax
from jax.sharding import Mesh, PartitionSpec as P

NZ = 8
PRE = ("z", "x")


def combine_pairs(earlier, later):
    return (earlier[0] * later[0], later[1] + later[0] * earlier[1])


def local_traces(spikes, decays):
    factor = jnp.broadcast_to(decays[None, :], spikes.shape)
    source = (1.0 - decays)[None, :] * spikes.astype(jnp.float32)
    return lax.associative_scan(combine_pairs, (factor, source), axis=0)


def pre_size():
    return lax.axis_size("z") * lax.axis_size("x")


def pre_index():
    return lax.axis_index("z") * lax.axis_size("x") + lax.axis_index("x")


def owned_errors(spikes, readout_weight, targets):
    npre = pre_size()
    b = pre_index()
    partial_logits = jnp.dot(
        spikes.astype(jnp.bfloat16), readout_weight, preferred_element_type=jnp.float32
    )
    rows = partial_logits.shape[0] // npre
    pieces = lax.all_to_all(partial_logits, PRE, 0, 0, tiled=True)
    logits = pieces.reshape(npre, rows, -1).sum(0)
    class_prob = jax.nn.softmax(logits, axis=-1)
    classes = lax.broadcasted_iota(jnp.int32, logits.shape, 1)
    mine = lax.dynamic_slice_in_dim(targets, b * rows, rows, 0)
    onehot = (mine[:, None] == classes).astype(jnp.float32)
    return (class_prob - onehot).astype(jnp.bfloat16)


def route_errors(errors, ntm, npre, deriv_rows):
    rows = errors.shape[0]
    tstep = rows * npre
    per = deriv_rows // rows
    perm = []
    for a in range(ntm):
        for b in range(npre):
            start = tstep * a + rows * b
            dst_b = start // deriv_rows
            dst_a = (start % deriv_rows) // rows
            perm.append((a * npre + b, dst_a * npre + dst_b))
    moved = lax.ppermute(errors, ("tm",) + PRE, perm)
    assert per == ntm
    return lax.all_gather(moved, "tm", axis=0, tiled=True)


def ring_gather(block, axis, count):
    index = lax.axis_index(axis)
    fwd = [(i, (i + 1) % count) for i in range(count)]
    bwd = [(i, (i - 1) % count) for i in range(count)]
    out = jnp.zeros((count,) + block.shape, block.dtype)
    out = lax.dynamic_update_slice_in_dim(out, block[None], index, 0)
    f = block
    b = block
    for s in range(1, count // 2 + 1):
        f = lax.ppermute(f, axis, fwd)
        out = lax.dynamic_update_slice_in_dim(out, f[None], (index - s) % count, 0)
        if s < count - count // 2:
            b = lax.ppermute(b, axis, bwd)
            out = lax.dynamic_update_slice_in_dim(out, b[None], (index + s) % count, 0)
    return out.reshape((count * block.shape[0],) + block.shape[1:])


def ring_stage(block, axis, count, fwd, bwd):
    coord = lax.axis_index(axis)
    pieces = [None] * count
    pieces[0] = block
    f = block
    r = block
    for s in range(1, count // 2 + 1):
        f = lax.ppermute(f, axis, fwd)
        pieces[count - s] = f
        if s < count - count // 2:
            r = lax.ppermute(r, axis, bwd)
            pieces[s] = r
    stacked = jnp.stack(pieces + pieces, 0)
    return lax.dynamic_slice_in_dim(stacked, (count - coord) % count, count, 0)


def weighted_gather(weighted):
    nz = lax.axis_size("z")
    nx = lax.axis_size("x")
    half = weighted.shape[1] // 2
    rows = nz * nx * weighted.shape[0]
    first = lax.all_gather(weighted[:, :half], "x", axis=0, tiled=True)
    first = lax.all_gather(first, "z", axis=0, tiled=True)
    zf = [(i, (i + 1) % nz) for i in range(nz)]
    zb = [(i, (i - 1) % nz) for i in range(nz)]
    xf = [(i, (i + 1) % nx) for i in range(nx)]
    xb = [(i, (i - 1) % nx) for i in range(nx)]
    second = ring_stage(ring_stage(weighted[:, half:], "z", nz, zf, zb), "x", nx, xf, xb)
    second = jnp.swapaxes(second, 0, 1)
    return first, second.reshape(rows, -1)


def shards(spikes, trace_decay, pseudo_deriv, readout_weight, feedback_weight, targets):
    ntm = lax.axis_size("tm")
    npre = pre_size()
    a = lax.axis_index("tm")

    errors = owned_errors(spikes, readout_weight, targets)
    err_rows = route_errors(errors, ntm, npre, pseudo_deriv.shape[0])
    signal = lax.dot_general(
        err_rows, feedback_weight, (((1,), (1,)), ((), ())), preferred_element_type=jnp.float32
    )
    weighted = (signal * pseudo_deriv.astype(jnp.float32)).astype(jnp.bfloat16)
    left_all, right_all = weighted_gather(weighted)

    powers, states = local_traces(spikes, trace_decay)
    ends = lax.all_gather(states[-1], "tm", axis=0)
    span = powers[-1]

    def step(k, carry):
        return jnp.where(k < a, span * carry + ends[k], carry)

    incoming = lax.fori_loop(0, ntm, step, jnp.zeros_like(trace_decay))
    traces = (states + powers * incoming[None, :]).astype(jnp.bfloat16)
    traces_all = ring_gather(traces, "tm", ntm)

    left = outer_sum(traces_all, left_all)
    right = outer_sum(traces_all, right_all)
    return jnp.concatenate([left, right], 1)


def outer_sum(left_rows, right_rows):
    return lax.dot_general(
        left_rows, right_rows, (((0,), (0,)), ((), ())), preferred_element_type=jnp.float32
    )


def solution(mesh):
    ntm, npre = mesh.devices.shape
    assert npre % NZ == 0
    plane = Mesh(mesh.devices.reshape(ntm, NZ, npre // NZ), ("tm",) + PRE)
    placed = (P("tm", PRE), P(PRE), P(PRE, "tm"), P(PRE, None), P("tm", None), P("tm"))
    return jax.shard_map(
        shards, mesh=plane, in_specs=placed, out_specs=P(PRE, "tm"), check_vma=False
    )
```

```python
import jax
import jax.numpy as jnp
from jax import lax
from jax.sharding import Mesh, PartitionSpec as P

NZ = 8
PRE = ("z", "x")


def combine_pairs(earlier, later):
    return (earlier[0] * later[0], later[1] + later[0] * earlier[1])


def local_traces(spikes, decays):
    factor = jnp.broadcast_to(decays[None, :], spikes.shape)
    source = (1.0 - decays)[None, :] * spikes.astype(jnp.float32)
    return lax.associative_scan(combine_pairs, (factor, source), axis=0)


def pre_size():
    return lax.axis_size("z") * lax.axis_size("x")


def pre_index():
    return lax.axis_index("z") * lax.axis_size("x") + lax.axis_index("x")


def owned_errors(spikes, readout_weight, targets):
    npre = pre_size()
    b = pre_index()
    partial_logits = jnp.dot(
        spikes.astype(jnp.bfloat16), readout_weight, preferred_element_type=jnp.float32
    )
    rows = partial_logits.shape[0] // npre
    pieces = lax.all_to_all(partial_logits, PRE, 0, 0, tiled=True)
    logits = pieces.reshape(npre, rows, -1).sum(0)
    class_prob = jax.nn.softmax(logits, axis=-1)
    classes = lax.broadcasted_iota(jnp.int32, logits.shape, 1)
    mine = lax.dynamic_slice_in_dim(targets, b * rows, rows, 0)
    onehot = (mine[:, None] == classes).astype(jnp.float32)
    return (class_prob - onehot).astype(jnp.bfloat16)


def route_errors(errors, ntm, npre, deriv_rows):
    rows = errors.shape[0]
    tstep = rows * npre
    per = deriv_rows // rows
    perm = []
    for a in range(ntm):
        for b in range(npre):
            start = tstep * a + rows * b
            dst_b = start // deriv_rows
            dst_a = (start % deriv_rows) // rows
            perm.append((a * npre + b, dst_a * npre + dst_b))
    moved = lax.ppermute(errors, ("tm",) + PRE, perm)
    assert per == ntm
    return lax.all_gather(moved, "tm", axis=0, tiled=True)


def ring_stage(block, axis, count, fwd, bwd):
    coord = lax.axis_index(axis)
    pieces = [None] * count
    pieces[0] = block
    f = block
    r = block
    for s in range(1, count // 2 + 1):
        f = lax.ppermute(f, axis, fwd)
        pieces[count - s] = f
        if s < count - count // 2:
            r = lax.ppermute(r, axis, bwd)
            pieces[s] = r
    stacked = jnp.stack(pieces + pieces, 0)
    return lax.dynamic_slice_in_dim(stacked, (count - coord) % count, count, 0)


def weighted_gather(weighted):
    nz = lax.axis_size("z")
    nx = lax.axis_size("x")
    half = weighted.shape[1] // 2
    rows = nz * nx * weighted.shape[0]
    zf = [(i, (i + 1) % nz) for i in range(nz)]
    zb = [(i, (i - 1) % nz) for i in range(nz)]
    xf = [(i, (i + 1) % nx) for i in range(nx)]
    xb = [(i, (i - 1) % nx) for i in range(nx)]
    first = ring_stage(weighted[:, :half], "x", nx, xf, xb)
    first = lax.all_gather(first.reshape(-1, half), "z", axis=0, tiled=True)
    second = ring_stage(ring_stage(weighted[:, half:], "z", nz, zf, zb), "x", nx, xf, xb)
    second = jnp.swapaxes(second, 0, 1)
    return first, second.reshape(rows, -1)


def shards(spikes, trace_decay, pseudo_deriv, readout_weight, feedback_weight, targets):
    ntm = lax.axis_size("tm")
    npre = pre_size()
    a = lax.axis_index("tm")

    errors = owned_errors(spikes, readout_weight, targets)
    err_rows = route_errors(errors, ntm, npre, pseudo_deriv.shape[0])
    signal = lax.dot_general(
        err_rows, feedback_weight, (((1,), (1,)), ((), ())), preferred_element_type=jnp.float32
    )
    weighted = (signal * pseudo_deriv.astype(jnp.float32)).astype(jnp.bfloat16)
    left_all, right_all = weighted_gather(weighted)

    powers, states = local_traces(spikes, trace_decay)
    ends = lax.all_gather(states[-1], "tm", axis=0)
    span = powers[-1]

    def step(k, carry):
        return jnp.where(k < a, span * carry + ends[k], carry)

    incoming = lax.fori_loop(0, ntm, step, jnp.zeros_like(trace_decay))
    traces = (states + powers * incoming[None, :]).astype(jnp.bfloat16)
    traces_all = lax.all_gather(traces, "tm", axis=0, tiled=True)

    left = outer_sum(traces_all, left_all)
    right = outer_sum(traces_all, right_all)
    return jnp.concatenate([left, right], 1)


def outer_sum(left_rows, right_rows):
    return lax.dot_general(
        left_rows, right_rows, (((0,), (0,)), ((), ())), preferred_element_type=jnp.float32
    )


def solution(mesh):
    ntm, npre = mesh.devices.shape
    assert npre % NZ == 0
    plane = Mesh(mesh.devices.reshape(ntm, NZ, npre // NZ), ("tm",) + PRE)
    placed = (P("tm", PRE), P(PRE), P(PRE, "tm"), P(PRE, None), P("tm", None), P("tm"))
    return jax.shard_map(
        shards, mesh=plane, in_specs=placed, out_specs=P(PRE, "tm"), check_vma=False
    )
```

```python
import jax
import jax.numpy as jnp
from jax import lax
from jax.sharding import Mesh, PartitionSpec as P

NZ = 8
PRE = ("z", "x")


def combine_pairs(earlier, later):
    return (earlier[0] * later[0], later[1] + later[0] * earlier[1])


def local_traces(spikes, decays):
    factor = jnp.broadcast_to(decays[None, :], spikes.shape)
    source = (1.0 - decays)[None, :] * spikes.astype(jnp.float32)
    return lax.associative_scan(combine_pairs, (factor, source), axis=0)


def pre_size():
    return lax.axis_size("z") * lax.axis_size("x")


def pre_index():
    return lax.axis_index("z") * lax.axis_size("x") + lax.axis_index("x")


def owned_errors(partial_logits, targets, spikes):
    npre = pre_size()
    b = pre_index()
    rows = partial_logits.shape[0] // npre
    pieces = lax.all_to_all(partial_logits, PRE, 0, 0, tiled=True)
    logits = pieces.reshape(npre, rows, -1).sum(0)
    class_prob = jax.nn.softmax(logits, axis=-1)
    classes = lax.broadcasted_iota(jnp.int32, logits.shape, 1)
    mine = lax.dynamic_slice_in_dim(targets, b * rows, rows, 0)
    onehot = (mine[:, None] == classes).astype(jnp.float32)
    return (class_prob - onehot).astype(jnp.bfloat16), spikes


def route_errors(errors, ntm, npre, deriv_rows):
    rows = errors.shape[0]
    tstep = rows * npre
    per = deriv_rows // rows
    perm = []
    for a in range(ntm):
        for b in range(npre):
            start = tstep * a + rows * b
            dst_b = start // deriv_rows
            dst_a = (start % deriv_rows) // rows
            perm.append((a * npre + b, dst_a * npre + dst_b))
    moved = lax.ppermute(errors, ("tm",) + PRE, perm)
    assert per == ntm
    return lax.all_gather(moved, "tm", axis=0, tiled=True)


def ring_stage(block, axis, count, fwd, bwd):
    coord = lax.axis_index(axis)
    pieces = [None] * count
    pieces[0] = block
    f = block
    r = block
    for s in range(1, count // 2 + 1):
        f = lax.ppermute(f, axis, fwd)
        pieces[count - s] = f
        if s < count - count // 2:
            r = lax.ppermute(r, axis, bwd)
            pieces[s] = r
    stacked = jnp.stack(pieces + pieces, 0)
    return lax.dynamic_slice_in_dim(stacked, (count - coord) % count, count, 0)


def weighted_gather(weighted):
    nz = lax.axis_size("z")
    nx = lax.axis_size("x")
    half = weighted.shape[1] // 2
    zf = [(i, (i + 1) % nz) for i in range(nz)]
    zb = [(i, (i - 1) % nz) for i in range(nz)]
    xf = [(i, (i + 1) % nx) for i in range(nx)]
    xb = [(i, (i - 1) % nx) for i in range(nx)]
    group = ring_stage(weighted, "x", nx, xf, xb)
    first = lax.all_gather(group[..., :half].reshape(-1, half), "z", axis=0, tiled=True)
    second = ring_stage(group[..., half:], "z", nz, zf, zb)
    return first, second.reshape(first.shape[0], -1)


def shards(spikes, trace_decay, pseudo_deriv, readout_weight, feedback_weight, targets):
    ntm = lax.axis_size("tm")
    npre = pre_size()
    a = lax.axis_index("tm")

    partial_logits = jnp.dot(
        spikes.astype(jnp.bfloat16), readout_weight, preferred_element_type=jnp.float32
    )
    errors, spikes = owned_errors(partial_logits, targets, spikes)
    err_rows = route_errors(errors, ntm, npre, pseudo_deriv.shape[0])
    signal = lax.dot_general(
        err_rows, feedback_weight, (((1,), (1,)), ((), ())), preferred_element_type=jnp.float32
    )
    weighted = (signal * pseudo_deriv.astype(jnp.float32)).astype(jnp.bfloat16)
    left_all, right_all = weighted_gather(weighted)

    powers, states = local_traces(spikes, trace_decay)
    ends = lax.all_gather(states[-1], "tm", axis=0)
    span = powers[-1]

    incoming = jnp.zeros_like(trace_decay)
    for k in range(ntm - 1):
        incoming = jnp.where(k < a, span * incoming + ends[k], incoming)
    traces = (states + powers * incoming[None, :]).astype(jnp.bfloat16)
    traces_all = lax.all_gather(traces, "tm", axis=0, tiled=True)

    left = outer_sum(traces_all, left_all)
    right = outer_sum(traces_all, right_all)
    return jnp.concatenate([left, right], 1)


def outer_sum(left_rows, right_rows):
    return lax.dot_general(
        left_rows, right_rows, (((0,), (0,)), ((), ())), preferred_element_type=jnp.float32
    )


def solution(mesh):
    ntm, npre = mesh.devices.shape
    assert npre % NZ == 0
    plane = Mesh(mesh.devices.reshape(ntm, NZ, npre // NZ), ("tm",) + PRE)
    placed = (P("tm", PRE), P(PRE), P(PRE, "tm"), P(PRE, None), P("tm", None), P("tm"))
    return jax.shard_map(
        shards, mesh=plane, in_specs=placed, out_specs=P(PRE, "tm"), check_vma=False
    )
```

```python
import jax
import jax.numpy as jnp
from jax import lax
from jax.sharding import PartitionSpec as P


def combine_pairs(earlier, later):
    return (earlier[0] * later[0], later[1] + later[0] * earlier[1])


def local_traces(spikes, decays):
    factor = jnp.broadcast_to(decays[None, :], spikes.shape)
    source = (1.0 - decays)[None, :] * spikes.astype(jnp.float32)
    return lax.associative_scan(combine_pairs, (factor, source), axis=0)


def owned_errors(spikes, readout_weight, targets):
    npre = lax.axis_size("pre")
    b = lax.axis_index("pre")
    partial_logits = jnp.dot(
        spikes.astype(jnp.bfloat16), readout_weight, preferred_element_type=jnp.float32
    )
    rows = partial_logits.shape[0] // npre
    pieces = lax.all_to_all(partial_logits, "pre", 0, 0, tiled=True)
    logits = pieces.reshape(npre, rows, -1).sum(0)
    class_prob = jax.nn.softmax(logits, axis=-1)
    classes = lax.broadcasted_iota(jnp.int32, logits.shape, 1)
    mine = lax.dynamic_slice_in_dim(targets, b * rows, rows, 0)
    onehot = (mine[:, None] == classes).astype(jnp.float32)
    return (class_prob - onehot).astype(jnp.bfloat16)


def ring_gather(block, axis, count):
    index = lax.axis_index(axis)
    fwd = [(i, (i + 1) % count) for i in range(count)]
    bwd = [(i, (i - 1) % count) for i in range(count)]
    out = jnp.zeros((count,) + block.shape, block.dtype)
    out = lax.dynamic_update_slice_in_dim(out, block[None], index, 0)
    f = block
    b = block
    for s in range(1, count // 2 + 1):
        f = lax.ppermute(f, axis, fwd)
        out = lax.dynamic_update_slice_in_dim(out, f[None], (index - s) % count, 0)
        if s < count - count // 2:
            b = lax.ppermute(b, axis, bwd)
            out = lax.dynamic_update_slice_in_dim(out, b[None], (index + s) % count, 0)
    return out.reshape((count * block.shape[0],) + block.shape[1:])


def shards(spikes, trace_decay, pseudo_deriv, readout_weight, feedback_weight, targets):
    ntm = lax.axis_size("tm")
    a = lax.axis_index("tm")

    derivs_all = lax.all_gather(pseudo_deriv, "pre", axis=0, tiled=True)

    errors = owned_errors(spikes, readout_weight, targets)
    errors_block = lax.all_gather(errors, "pre", axis=0, tiled=True)

    powers, states = local_traces(spikes, trace_decay)
    ends = lax.all_gather(states[-1], "tm", axis=0)
    span = powers[-1]
    incoming = jnp.zeros_like(trace_decay)
    for k in range(ntm - 1):
        incoming = jnp.where(k < a, span * incoming + ends[k], incoming)
    traces = (states + powers * incoming[None, :]).astype(jnp.bfloat16)
    traces_all = lax.all_gather(traces, "tm", axis=0, tiled=True)

    errors_all = ring_gather(errors_block, "tm", ntm)
    signal = lax.dot_general(
        errors_all, feedback_weight, (((1,), (1,)), ((), ())), preferred_element_type=jnp.float32
    )
    weighted_all = (signal * derivs_all.astype(jnp.float32)).astype(jnp.bfloat16)

    return lax.dot_general(
        traces_all, weighted_all, (((0,), (0,)), ((), ())), preferred_element_type=jnp.float32
    )


def solution(mesh):
    placed = (P("tm", "pre"), P("pre"), P("pre", "tm"), P("pre", None), P("tm", None), P("tm"))
    return jax.shard_map(
        shards, mesh=mesh, in_specs=placed, out_specs=P("pre", "tm"), check_vma=False
    )
```

```python
import jax
import jax.numpy as jnp
from jax import lax
from jax.sharding import PartitionSpec as P

NZ = 8


def combine_pairs(earlier, later):
    return (earlier[0] * later[0], later[1] + later[0] * earlier[1])


def local_traces(spikes, decays):
    factor = jnp.broadcast_to(decays[None, :], spikes.shape)
    source = (1.0 - decays)[None, :] * spikes.astype(jnp.float32)
    return lax.associative_scan(combine_pairs, (factor, source), axis=0)


def owned_errors(spikes, readout_weight, targets):
    npre = lax.axis_size("pre")
    b = lax.axis_index("pre")
    partial_logits = jnp.dot(
        spikes.astype(jnp.bfloat16), readout_weight, preferred_element_type=jnp.float32
    )
    rows = partial_logits.shape[0] // npre
    pieces = lax.all_to_all(partial_logits, "pre", 0, 0, tiled=True)
    logits = pieces.reshape(npre, rows, -1).sum(0)
    class_prob = jax.nn.softmax(logits, axis=-1)
    classes = lax.broadcasted_iota(jnp.int32, logits.shape, 1)
    mine = lax.dynamic_slice_in_dim(targets, b * rows, rows, 0)
    onehot = (mine[:, None] == classes).astype(jnp.float32)
    return (class_prob - onehot).astype(jnp.bfloat16)


def route_errors(errors, ntm, npre, deriv_rows):
    rows = errors.shape[0]
    tstep = rows * npre
    per = deriv_rows // rows
    perm = []
    for a in range(ntm):
        for b in range(npre):
            start = tstep * a + rows * b
            dst_b = start // deriv_rows
            dst_a = (start % deriv_rows) // rows
            perm.append((a * npre + b, dst_a * npre + dst_b))
    moved = lax.ppermute(errors, ("tm", "pre"), perm)
    assert per == ntm
    return lax.all_gather(moved, "tm", axis=0, tiled=True)


def ring_stage(block, coord, count, fwd, bwd):
    out = jnp.zeros((count,) + block.shape, block.dtype)
    out = lax.dynamic_update_slice_in_dim(out, block[None], coord, 0)
    f = block
    r = block
    for s in range(1, count // 2 + 1):
        f = lax.ppermute(f, "pre", fwd)
        out = lax.dynamic_update_slice_in_dim(out, f[None], (coord - s) % count, 0)
        if s < count - count // 2:
            r = lax.ppermute(r, "pre", bwd)
            out = lax.dynamic_update_slice_in_dim(out, r[None], (coord + s) % count, 0)
    return out


def plane_gather(block, nz, nx):
    b = lax.axis_index("pre")
    z = b // nx
    x = b % nx
    xf = [(zz * nx + xx, zz * nx + (xx + 1) % nx) for zz in range(nz) for xx in range(nx)]
    xb = [(zz * nx + xx, zz * nx + (xx - 1) % nx) for zz in range(nz) for xx in range(nx)]
    zf = [(zz * nx + xx, ((zz + 1) % nz) * nx + xx) for zz in range(nz) for xx in range(nx)]
    zb = [(zz * nx + xx, ((zz - 1) % nz) * nx + xx) for zz in range(nz) for xx in range(nx)]
    group = ring_stage(block, x, nx, xf, xb)
    full = ring_stage(group, z, nz, zf, zb)
    return full.reshape((nz * nx * block.shape[0],) + block.shape[1:])


def ring_gather(block, axis, count):
    index = lax.axis_index(axis)
    fwd = [(i, (i + 1) % count) for i in range(count)]
    bwd = [(i, (i - 1) % count) for i in range(count)]
    out = jnp.zeros((count,) + block.shape, block.dtype)
    out = lax.dynamic_update_slice_in_dim(out, block[None], index, 0)
    f = block
    b = block
    for s in range(1, count // 2 + 1):
        f = lax.ppermute(f, axis, fwd)
        out = lax.dynamic_update_slice_in_dim(out, f[None], (index - s) % count, 0)
        if s < count - count // 2:
            b = lax.ppermute(b, axis, bwd)
            out = lax.dynamic_update_slice_in_dim(out, b[None], (index + s) % count, 0)
    return out.reshape((count * block.shape[0],) + block.shape[1:])


def shards(spikes, trace_decay, pseudo_deriv, readout_weight, feedback_weight, targets):
    ntm = lax.axis_size("tm")
    a = lax.axis_index("tm")

    derivs_all = lax.all_gather(pseudo_deriv, "pre", axis=0, tiled=True)

    errors = owned_errors(spikes, readout_weight, targets)
    npre = lax.axis_size("pre")
    assert npre % NZ == 0
    err_rows = route_errors(errors, ntm, npre, pseudo_deriv.shape[0])

    powers, states = local_traces(spikes, trace_decay)
    ends = lax.all_gather(states[-1], "tm", axis=0)
    span = powers[-1]
    incoming = jnp.zeros_like(trace_decay)
    for k in range(ntm - 1):
        incoming = jnp.where(k < a, span * incoming + ends[k], incoming)
    traces = (states + powers * incoming[None, :]).astype(jnp.bfloat16)
    traces_all = ring_gather(traces, "tm", ntm)

    errors_all = plane_gather(err_rows, NZ, npre // NZ)
    signal = lax.dot_general(
        errors_all, feedback_weight, (((1,), (1,)), ((), ())), preferred_element_type=jnp.float32
    )
    weighted_all = (signal * derivs_all.astype(jnp.float32)).astype(jnp.bfloat16)

    return lax.dot_general(
        traces_all, weighted_all, (((0,), (0,)), ((), ())), preferred_element_type=jnp.float32
    )


def solution(mesh):
    placed = (P("tm", "pre"), P("pre"), P("pre", "tm"), P("pre", None), P("tm", None), P("tm"))
    return jax.shard_map(
        shards, mesh=mesh, in_specs=placed, out_specs=P("pre", "tm"), check_vma=False
    )
```

```python
import jax
import jax.numpy as jnp
from jax import lax
from jax.sharding import Mesh, PartitionSpec as P

NZ = 8
PRE = ("z", "x")


def combine_pairs(earlier, later):
    return (earlier[0] * later[0], later[1] + later[0] * earlier[1])


def local_traces(spikes, decays):
    factor = jnp.broadcast_to(decays[None, :], spikes.shape)
    source = (1.0 - decays)[None, :] * spikes.astype(jnp.float32)
    return lax.associative_scan(combine_pairs, (factor, source), axis=0)


def pre_size():
    return lax.axis_size("z") * lax.axis_size("x")


def pre_index():
    return lax.axis_index("z") * lax.axis_size("x") + lax.axis_index("x")


def owned_errors(spikes, readout_weight, targets):
    npre = pre_size()
    b = pre_index()
    partial_logits = jnp.dot(
        spikes.astype(jnp.bfloat16), readout_weight, preferred_element_type=jnp.float32
    )
    rows = partial_logits.shape[0] // npre
    pieces = lax.all_to_all(partial_logits, PRE, 0, 0, tiled=True)
    logits = pieces.reshape(npre, rows, -1).sum(0)
    class_prob = jax.nn.softmax(logits, axis=-1)
    classes = lax.broadcasted_iota(jnp.int32, logits.shape, 1)
    mine = lax.dynamic_slice_in_dim(targets, b * rows, rows, 0)
    onehot = (mine[:, None] == classes).astype(jnp.float32)
    return (class_prob - onehot).astype(jnp.bfloat16)


def route_errors(errors, ntm, npre, deriv_rows):
    rows = errors.shape[0]
    tstep = rows * npre
    per = deriv_rows // rows
    perm = []
    for a in range(ntm):
        for b in range(npre):
            start = tstep * a + rows * b
            dst_b = start // deriv_rows
            dst_a = (start % deriv_rows) // rows
            perm.append((a * npre + b, dst_a * npre + dst_b))
    moved = lax.ppermute(errors, ("tm",) + PRE, perm)
    assert per == ntm
    return lax.all_gather(moved, "tm", axis=0, tiled=True)


def ring_stage(block, axis, count, fwd, bwd):
    coord = lax.axis_index(axis)
    pieces = [None] * count
    pieces[0] = block
    f = block
    r = block
    for s in range(1, count // 2 + 1):
        f = lax.ppermute(f, axis, fwd)
        pieces[count - s] = f
        if s < count - count // 2:
            r = lax.ppermute(r, axis, bwd)
            pieces[s] = r
    stacked = jnp.stack(pieces + pieces, 0)
    return lax.dynamic_slice_in_dim(stacked, (count - coord) % count, count, 0)


def weighted_gather(weighted):
    nz = lax.axis_size("z")
    nx = lax.axis_size("x")
    half = weighted.shape[1] // 2
    rows = nz * nx * weighted.shape[0]
    zf = [(i, (i + 1) % nz) for i in range(nz)]
    zb = [(i, (i - 1) % nz) for i in range(nz)]
    xf = [(i, (i + 1) % nx) for i in range(nx)]
    xb = [(i, (i - 1) % nx) for i in range(nx)]
    first = ring_stage(weighted[:, :half], "x", nx, xf, xb)
    first, rest = lax.optimization_barrier((first, weighted[:, half:]))
    first = lax.all_gather(first.reshape(-1, half), "z", axis=0, tiled=True)
    second = ring_stage(ring_stage(rest, "z", nz, zf, zb), "x", nx, xf, xb)
    second = jnp.swapaxes(second, 0, 1)
    return first, second.reshape(rows, -1)


def shards(spikes, trace_decay, pseudo_deriv, readout_weight, feedback_weight, targets):
    ntm = lax.axis_size("tm")
    npre = pre_size()
    a = lax.axis_index("tm")

    errors = owned_errors(spikes, readout_weight, targets)

    powers, states = local_traces(spikes, trace_decay)
    spikes_all = lax.all_gather(spikes.astype(jnp.bfloat16), "tm", axis=0, tiled=True)
    spikes_all, errors = lax.optimization_barrier((spikes_all, errors))
    err_rows = route_errors(errors, ntm, npre, pseudo_deriv.shape[0])
    steps = spikes.shape[0]
    weights = jnp.concatenate([powers[steps - 2::-1], jnp.ones_like(powers[:1])], 0)
    weights = weights * (1.0 - trace_decay)[None, :]
    blocks = spikes_all.reshape(ntm, steps, -1).astype(jnp.float32)
    ends = jnp.sum(blocks * weights[None], axis=1)
    span = powers[-1]
    incoming = jnp.zeros_like(trace_decay)
    for k in range(ntm - 1):
        incoming = jnp.where(k < a, span * incoming + ends[k], incoming)
    traces = (states + powers * incoming[None, :]).astype(jnp.bfloat16)
    traces_all = lax.all_gather(traces, "tm", axis=0, tiled=True)
    signal = lax.dot_general(
        err_rows, feedback_weight, (((1,), (1,)), ((), ())), preferred_element_type=jnp.float32
    )
    weighted = (signal * pseudo_deriv.astype(jnp.float32)).astype(jnp.bfloat16)
    left_all, right_all = weighted_gather(weighted)

    left = outer_sum(traces_all, left_all)
    right = outer_sum(traces_all, right_all)
    return jnp.concatenate([left, right], 1)


def outer_sum(left_rows, right_rows):
    return lax.dot_general(
        left_rows, right_rows, (((0,), (0,)), ((), ())), preferred_element_type=jnp.float32
    )


def solution(mesh):
    ntm, npre = mesh.devices.shape
    assert npre % NZ == 0
    plane = Mesh(mesh.devices.reshape(ntm, NZ, npre // NZ), ("tm",) + PRE)
    placed = (P("tm", PRE), P(PRE), P(PRE, "tm"), P(PRE, None), P("tm", None), P("tm"))
    return jax.shard_map(
        shards, mesh=plane, in_specs=placed, out_specs=P(PRE, "tm"), check_vma=False
    )
```

```python
import jax
import jax.numpy as jnp
from jax import lax
from jax.sharding import Mesh, PartitionSpec as P

TM = ("y", "core")


def tm_size():
    return lax.axis_size("y") * lax.axis_size("core")


def tm_index():
    return lax.axis_index("y") * lax.axis_size("core") + lax.axis_index("core")


def combine_pairs(earlier, later):
    return (earlier[0] * later[0], later[1] + later[0] * earlier[1])


def local_traces(spikes, decays):
    factor = jnp.broadcast_to(decays[None, :], spikes.shape)
    source = (1.0 - decays)[None, :] * spikes.astype(jnp.float32)
    return lax.associative_scan(combine_pairs, (factor, source), axis=0)


def owned_errors(spikes, readout_weight, targets):
    npre = lax.axis_size("pre")
    b = lax.axis_index("pre")
    partial_logits = jnp.dot(
        spikes.astype(jnp.bfloat16), readout_weight, preferred_element_type=jnp.float32
    )
    rows = partial_logits.shape[0] // npre
    pieces = lax.all_to_all(partial_logits, "pre", 0, 0, tiled=True)
    logits = pieces.reshape(npre, rows, -1).sum(0)
    class_prob = jax.nn.softmax(logits, axis=-1)
    classes = lax.broadcasted_iota(jnp.int32, logits.shape, 1)
    mine = lax.dynamic_slice_in_dim(targets, b * rows, rows, 0)
    onehot = (mine[:, None] == classes).astype(jnp.float32)
    return (class_prob - onehot).astype(jnp.bfloat16)


def route_errors(errors, ntm, npre, deriv_rows):
    rows = errors.shape[0]
    tstep = rows * npre
    per = deriv_rows // rows
    perm = []
    for a in range(ntm):
        for b in range(npre):
            start = tstep * a + rows * b
            dst_b = start // deriv_rows
            dst_a = (start % deriv_rows) // rows
            perm.append((a * npre + b, dst_a * npre + dst_b))
    moved = lax.ppermute(errors, TM + ("pre",), perm)
    assert per == ntm
    pair = lax.all_gather(moved, "core", axis=0, tiled=True)
    return lax.all_gather(pair, "y", axis=0, tiled=True)


def ring_gather(block, axis, count):
    index = tm_index()
    fwd = [(i, (i + 1) % count) for i in range(count)]
    bwd = [(i, (i - 1) % count) for i in range(count)]
    out = jnp.zeros((count,) + block.shape, block.dtype)
    out = lax.dynamic_update_slice_in_dim(out, block[None], index, 0)
    f = block
    b = block
    for s in range(1, count // 2 + 1):
        f = lax.ppermute(f, axis, fwd)
        out = lax.dynamic_update_slice_in_dim(out, f[None], (index - s) % count, 0)
        if s < count - count // 2:
            b = lax.ppermute(b, axis, bwd)
            out = lax.dynamic_update_slice_in_dim(out, b[None], (index + s) % count, 0)
    return out.reshape((count * block.shape[0],) + block.shape[1:])


def shards(spikes, trace_decay, pseudo_deriv, readout_weight, feedback_weight, targets):
    ntm = tm_size()
    npre = lax.axis_size("pre")
    a = tm_index()

    errors = owned_errors(spikes, readout_weight, targets)
    err_rows = route_errors(errors, ntm, npre, pseudo_deriv.shape[0])
    powers, states = local_traces(spikes, trace_decay)
    end_state, err_rows = lax.optimization_barrier((states[-1], err_rows))
    ends = lax.all_gather(end_state, TM, axis=0)
    span = powers[-1]

    def step(k, carry):
        return jnp.where(k < a, span * carry + ends[k], carry)

    incoming = lax.fori_loop(0, ntm, step, jnp.zeros_like(trace_decay))
    traces = (states + powers * incoming[None, :]).astype(jnp.bfloat16)
    traces_all = ring_gather(traces, TM, ntm)
    signal = lax.dot_general(
        err_rows, feedback_weight, (((1,), (1,)), ((), ())), preferred_element_type=jnp.float32
    )
    weighted = (signal * pseudo_deriv.astype(jnp.float32)).astype(jnp.bfloat16)
    weighted_all = lax.all_gather(weighted, "pre", axis=0, tiled=True)

    return lax.dot_general(
        traces_all, weighted_all, (((0,), (0,)), ((), ())), preferred_element_type=jnp.float32
    )


def solution(mesh):
    ntm, npre = mesh.devices.shape
    split = Mesh(mesh.devices.reshape(ntm // 2, 2, npre), TM + ("pre",))
    placed = (P(TM, "pre"), P("pre"), P("pre", TM), P("pre", None), P(TM, None), P(TM))
    return jax.shard_map(
        shards, mesh=split, in_specs=placed, out_specs=P("pre", TM), check_vma=False
    )
```

```python
import jax
import jax.numpy as jnp
from jax import lax
from jax.sharding import PartitionSpec as P


def combine_pairs(earlier, later):
    return (earlier[0] * later[0], later[1] + later[0] * earlier[1])


def local_traces(spikes, decays):
    factor = jnp.broadcast_to(decays[None, :], spikes.shape)
    source = (1.0 - decays)[None, :] * spikes.astype(jnp.float32)
    return lax.associative_scan(combine_pairs, (factor, source), axis=0)


def owned_errors(spikes, readout_weight, targets):
    npre = lax.axis_size("pre")
    b = lax.axis_index("pre")
    partial_logits = jnp.dot(
        spikes.astype(jnp.bfloat16), readout_weight, preferred_element_type=jnp.float32
    )
    rows = partial_logits.shape[0] // npre
    tile = -(-rows // 8) * 8
    padded = jnp.pad(partial_logits.reshape(npre, rows, -1), ((0, 0), (0, tile - rows), (0, 0)))
    pieces = lax.all_to_all(padded, "pre", 0, 0, tiled=True)
    logits = pieces[:, :rows].sum(0)
    class_prob = jax.nn.softmax(logits, axis=-1)
    classes = lax.broadcasted_iota(jnp.int32, logits.shape, 1)
    mine = lax.dynamic_slice_in_dim(targets, b * rows, rows, 0)
    onehot = (mine[:, None] == classes).astype(jnp.float32)
    return (class_prob - onehot).astype(jnp.bfloat16)


def route_errors(errors, ntm, npre, deriv_rows):
    rows = errors.shape[0]
    tstep = rows * npre
    per = deriv_rows // rows
    perm = []
    for a in range(ntm):
        for b in range(npre):
            start = tstep * a + rows * b
            dst_b = start // deriv_rows
            dst_a = (start % deriv_rows) // rows
            perm.append((a * npre + b, dst_a * npre + dst_b))
    moved = lax.ppermute(errors, ("tm", "pre"), perm)
    assert per == ntm
    return lax.all_gather(moved, "tm", axis=0, tiled=True)


def ring_gather(block, axis, count):
    index = lax.axis_index(axis)
    fwd = [(i, (i + 1) % count) for i in range(count)]
    bwd = [(i, (i - 1) % count) for i in range(count)]
    out = jnp.zeros((count,) + block.shape, block.dtype)
    out = lax.dynamic_update_slice_in_dim(out, block[None], index, 0)
    f = block
    b = block
    for s in range(1, count // 2 + 1):
        f = lax.ppermute(f, axis, fwd)
        out = lax.dynamic_update_slice_in_dim(out, f[None], (index - s) % count, 0)
        if s < count - count // 2:
            b = lax.ppermute(b, axis, bwd)
            out = lax.dynamic_update_slice_in_dim(out, b[None], (index + s) % count, 0)
    return out.reshape((count * block.shape[0],) + block.shape[1:])


def shards(spikes, trace_decay, pseudo_deriv, readout_weight, feedback_weight, targets):
    ntm = lax.axis_size("tm")
    npre = lax.axis_size("pre")
    a = lax.axis_index("tm")

    errors = owned_errors(spikes, readout_weight, targets)
    err_rows = route_errors(errors, ntm, npre, pseudo_deriv.shape[0])
    signal = lax.dot_general(
        err_rows, feedback_weight, (((1,), (1,)), ((), ())), preferred_element_type=jnp.float32
    )
    weighted = (signal * pseudo_deriv.astype(jnp.float32)).astype(jnp.bfloat16)
    weighted_all = lax.all_gather(weighted, "pre", axis=0, tiled=True)

    powers, states = local_traces(spikes, trace_decay)
    ends = lax.all_gather(states[-1], "tm", axis=0)
    span = powers[-1]

    def step(k, carry):
        return jnp.where(k < a, span * carry + ends[k], carry)

    incoming = lax.fori_loop(0, ntm, step, jnp.zeros_like(trace_decay))
    traces = (states + powers * incoming[None, :]).astype(jnp.bfloat16)
    traces_all = ring_gather(traces, "tm", ntm)

    return lax.dot_general(
        traces_all, weighted_all, (((0,), (0,)), ((), ())), preferred_element_type=jnp.float32
    )


def solution(mesh):
    placed = (P("tm", "pre"), P("pre"), P("pre", "tm"), P("pre", None), P("tm", None), P("tm"))
    return jax.shard_map(
        shards, mesh=mesh, in_specs=placed, out_specs=P("pre", "tm"), check_vma=False
    )
```

```python
import jax
import jax.numpy as jnp
from jax import lax
from jax.sharding import PartitionSpec as P


def combine_pairs(earlier, later):
    return (earlier[0] * later[0], later[1] + later[0] * earlier[1])


def local_traces(spikes, decays):
    factor = jnp.broadcast_to(decays[None, :], spikes.shape)
    source = (1.0 - decays)[None, :] * spikes.astype(jnp.float32)
    return lax.associative_scan(combine_pairs, (factor, source), axis=0)


def owned_errors(spikes, readout_weight, targets):
    npre = lax.axis_size("pre")
    b = lax.axis_index("pre")
    rows = spikes.shape[0] // npre
    spike_pieces = spikes.astype(jnp.bfloat16).reshape(npre, rows, -1)
    partial_logits = lax.dot_general(
        spike_pieces, readout_weight, (((2,), (0,)), ((), ())), preferred_element_type=jnp.float32
    )
    pieces = lax.all_to_all(partial_logits, "pre", 0, 0, tiled=True)
    logits = pieces.sum(0)
    class_prob = jax.nn.softmax(logits, axis=-1)
    classes = lax.broadcasted_iota(jnp.int32, logits.shape, 1)
    mine = lax.dynamic_slice_in_dim(targets, b * rows, rows, 0)
    onehot = (mine[:, None] == classes).astype(jnp.float32)
    return (class_prob - onehot).astype(jnp.bfloat16)


def route_errors(errors, ntm, npre, deriv_rows):
    rows = errors.shape[0]
    tstep = rows * npre
    per = deriv_rows // rows
    perm = []
    for a in range(ntm):
        for b in range(npre):
            start = tstep * a + rows * b
            dst_b = start // deriv_rows
            dst_a = (start % deriv_rows) // rows
            perm.append((a * npre + b, dst_a * npre + dst_b))
    moved = lax.ppermute(errors, ("tm", "pre"), perm)
    assert per == ntm
    return lax.all_gather(moved, "tm", axis=0, tiled=True)


def ring_gather(block, axis, count):
    index = lax.axis_index(axis)
    fwd = [(i, (i + 1) % count) for i in range(count)]
    bwd = [(i, (i - 1) % count) for i in range(count)]
    out = jnp.zeros((count,) + block.shape, block.dtype)
    out = lax.dynamic_update_slice_in_dim(out, block[None], index, 0)
    f = block
    b = block
    for s in range(1, count // 2 + 1):
        f = lax.ppermute(f, axis, fwd)
        out = lax.dynamic_update_slice_in_dim(out, f[None], (index - s) % count, 0)
        if s < count - count // 2:
            b = lax.ppermute(b, axis, bwd)
            out = lax.dynamic_update_slice_in_dim(out, b[None], (index + s) % count, 0)
    return out.reshape((count * block.shape[0],) + block.shape[1:])


def shards(spikes, trace_decay, pseudo_deriv, readout_weight, feedback_weight, targets):
    ntm = lax.axis_size("tm")
    npre = lax.axis_size("pre")
    a = lax.axis_index("tm")

    errors = owned_errors(spikes, readout_weight, targets)
    err_rows = route_errors(errors, ntm, npre, pseudo_deriv.shape[0])
    signal = lax.dot_general(
        err_rows, feedback_weight, (((1,), (1,)), ((), ())), preferred_element_type=jnp.float32
    )
    weighted = (signal * pseudo_deriv.astype(jnp.float32)).astype(jnp.bfloat16)
    weighted_all = lax.all_gather(weighted, "pre", axis=0, tiled=True)

    powers, states = local_traces(spikes, trace_decay)
    ends = lax.all_gather(states[-1], "tm", axis=0)
    span = powers[-1]

    def step(k, carry):
        return jnp.where(k < a, span * carry + ends[k], carry)

    incoming = lax.fori_loop(0, ntm, step, jnp.zeros_like(trace_decay))
    traces = (states + powers * incoming[None, :]).astype(jnp.bfloat16)
    traces_all = ring_gather(traces, "tm", ntm)

    return lax.dot_general(
        traces_all, weighted_all, (((0,), (0,)), ((), ())), preferred_element_type=jnp.float32
    )


def solution(mesh):
    placed = (P("tm", "pre"), P("pre"), P("pre", "tm"), P("pre", None), P("tm", None), P("tm"))
    return jax.shard_map(
        shards, mesh=mesh, in_specs=placed, out_specs=P("pre", "tm"), check_vma=False
    )
```
